256 devices in a mesh: seq: 16 (over x_lo, y, core), tensor: 16 (over z, x_hi).
Axes of the slice: x: 4 (x_hi: 2, x_lo: 2; x = x_hi * 2 + x_lo), y: 4, z: 8, core: 2. Of those that a mesh axis runs over, the one named last changes fastest.
Arguments:
- tokens: bfloat16 [4096, 8192], P('tensor', 'seq'), may hold values from -6 to 6
- in_weight: bfloat16 [3, 8192, 8192], P(None, 'seq', 'tensor'), may hold values from -0.0625 to 0.0625
- filters: float32 [512, 128], P('tensor'), may hold values from -0.5 to 0.5
- skip_gain: float32 [8192], P('tensor'), may hold values from -4 to 4
- out_weight: bfloat16 [8192, 8192], P('tensor', 'seq'), may hold values from -0.0625 to 0.0625
Outputs:
- mixed: bfloat16 [4096, 8192], P('seq', 'tensor')
The draws below stay inside these ranges and needn't reach their ends.
All inputs are finite; a program needn't handle non-finite values.
Results may differ from the reference program's by a relative error of at most 0.035.
Values may be sent and summed in bfloat16 or wider, within the bound.
No kernel may reach another device: no remote copies, remote signals or barrier semaphores. Data moves between devices by JAX's collectives and lax.ppermute only.
A program may use at most 128 MiB of HBM per device.

```python
import jax
import jax.numpy as jnp
from jax import lax

D = 8192
KSIZE = 128
GROUP_SIZE = 16
TOKENS = 4096
GROUPS = 512
N_SEQ = 16
N_TENSOR = 16


def steps_of(stream_key, shape, cuts, low, top_value):
    def one(dim, parts):
        heights = jax.random.uniform(jax.random.fold_in(jax.random.fold_in(stream_key, 6), dim), (parts,), jnp.float32, low / len(cuts), top_value / len(cuts))
        return jnp.repeat(jnp.exp(heights), shape[dim] // parts).reshape((-1,) + (1,) * (len(shape) - dim - 1))

    level = one(*cuts[0])
    for cut in cuts[1:]:
        level = level * one(*cut)
    return level


def gaussian(own_key, shape, spread, reach, split=(), kind=jnp.bfloat16):
    drawn = spread * jax.random.normal(own_key, shape, jnp.float32)
    if split:
        drawn = drawn * steps_of(own_key, shape, split, -0.22, 0.18)
    return jnp.clip(drawn, -reach, reach).astype(kind)


def setup_inputs(seed: int = 0) -> dict:
    arg_keys = jax.random.split(jax.random.key(seed), 6)
    return {
        "tokens": gaussian(arg_keys[0], (TOKENS, D), 1.0, 6.0, ((0, 16), (1, 16))),
        "in_weight": gaussian(arg_keys[1], (3, D, D), D ** -0.5, 0.0625, ((1, 16), (2, 16))),
        "filters": gaussian(arg_keys[2], (GROUPS, KSIZE), 0.09, 0.5, ((0, 16),), jnp.float32),
        "skip_gain": gaussian(arg_keys[3], (D,), 1.0, 4.0, ((0, 16),), jnp.float32),
        "out_weight": gaussian(arg_keys[4], (D, D), D ** -0.5, 0.0625, ((0, 16), (1, 16))),
    }


def causal_taps(product, filters, rows, width):
    padded = jnp.pad(product, ((KSIZE - 1, 0), (0, 0)))
    per_channel = jnp.repeat(filters, GROUP_SIZE, axis=0)

    def add_tap(tap_index, accum):
        start = (KSIZE - 1 - tap_index).astype(jnp.int32)
        shifted = lax.dynamic_slice_in_dim(padded, start, rows, 0)
        column = lax.dynamic_slice_in_dim(per_channel, tap_index.astype(jnp.int32), 1, 1)[:, 0]
        return accum + shifted * column[None, :]

    start_sum = jnp.zeros((rows, width), product.dtype)
    return lax.fori_loop(jnp.int32(0), jnp.int32(KSIZE), add_tap, start_sum)


def reference(tokens, in_weight, filters, skip_gain, out_weight):
    feat_block = D // N_SEQ
    total = jnp.zeros((3, TOKENS, D), jnp.float32)
    for block_index in range(N_SEQ):
        low = block_index * feat_block
        rows_part = tokens[:, low:low + feat_block].astype(jnp.float32)
        weight_part = in_weight[:, low:low + feat_block, :].astype(jnp.float32)
        partial_sum = jnp.einsum('rf,sfc->src', rows_part, weight_part)
        rounded = lax.optimization_barrier(partial_sum.astype(jnp.bfloat16))
        total = total + rounded.astype(jnp.float32)
    streams = total.astype(jnp.bfloat16)
    query_rows = streams[0].astype(jnp.float32)
    key_rows = streams[1].astype(jnp.float32)
    value_rows = streams[2].astype(jnp.float32)
    product = (key_rows * value_rows).astype(jnp.bfloat16).astype(jnp.float32)
    conv = causal_taps(product, filters, TOKENS, D)
    conv = conv + skip_gain[None, :] * product
    gated = (query_rows * conv).astype(jnp.bfloat16)
    chan_block = D // N_TENSOR
    accum = jnp.zeros((TOKENS, D), jnp.float32)
    for block_index in range(N_TENSOR):
        low = block_index * chan_block
        part_out = jnp.dot(gated[:, low:low + chan_block].astype(jnp.float32), out_weight[low:low + chan_block, :].astype(jnp.float32))
        rounded = lax.optimization_barrier(part_out.astype(jnp.bfloat16))
        accum = accum + rounded.astype(jnp.float32)
    return accum.astype(jnp.bfloat16)
```

```python
import jax
import jax.numpy as jnp
from jax import lax
from jax.sharding import PartitionSpec as P


def from_behind(x, axis, by):
    peers = lax.axis_size(axis)
    pairs = [(i, i + by) for i in range(peers) if 0 <= i + by < peers]
    return lax.ppermute(x, axis, pairs)


def toeplitz_conv(ext, filters):
    groups, taps = filters.shape
    rows, channels = ext.shape
    tok = rows - (taps - 1)
    gw = channels // groups
    nblk = tok // taps
    extp = jnp.concatenate([ext, jnp.zeros((1, channels), ext.dtype)], axis=0)
    blocks = extp.reshape(nblk + 1, taps, groups, gw)
    win = jnp.concatenate([blocks[:-1], blocks[1:]], axis=1)
    w = jnp.pad(filters[:, ::-1], ((0, 0), (0, taps + 1)))
    toe = jnp.tile(w, (1, taps))[:, : taps * 2 * taps].reshape(groups, taps, 2 * taps)
    hi = toe.astype(jnp.bfloat16)
    lo = (toe - hi.astype(jnp.float32)).astype(jnp.bfloat16)
    out = jnp.einsum("gts,isgc->itgc", hi, win, preferred_element_type=jnp.float32)
    out = out + jnp.einsum("gts,isgc->itgc", lo, win, preferred_element_type=jnp.float32)
    return out.reshape(tok, channels)


def per_device(tokens, in_weight, filters, skip_gain, out_weight):
    gathered = lax.all_gather(tokens, "tensor", axis=0, tiled=True)
    tok_dev = gathered.shape[0] // lax.axis_size("seq")
    channels = in_weight.shape[2]
    taps_count = filters.shape[1]
    group_width = channels // filters.shape[0]
    summed = lax.psum_scatter(
        jnp.einsum("rf,sfc->rsc", gathered, in_weight, preferred_element_type=jnp.float32).astype(
            jnp.bfloat16
        ),
        "seq",
        scatter_dimension=0,
        tiled=True,
    ).astype(jnp.float32)
    query_rows = summed[:, 0].astype(jnp.bfloat16)
    key_rows = summed[:, 1].astype(jnp.bfloat16)
    value_rows = summed[:, 2].astype(jnp.bfloat16)
    product = (key_rows.astype(jnp.float32) * value_rows.astype(jnp.float32)).astype(jnp.bfloat16)
    previous = from_behind(product[tok_dev - (taps_count - 1) :], "seq", 1)
    product_f = product.astype(jnp.float32)
    extended = jnp.concatenate([previous, product], axis=0)
    conv = toeplitz_conv(extended, filters)
    conv = conv + skip_gain[None, :] * product_f
    gated = (query_rows.astype(jnp.float32) * conv).astype(jnp.bfloat16)
    partial_out = jnp.dot(
        gated,
        lax.all_gather(out_weight, "seq", axis=1, tiled=True),
        preferred_element_type=jnp.float32,
    )
    return lax.psum_scatter(
        partial_out.astype(jnp.bfloat16), "tensor", scatter_dimension=1, tiled=True
    )


def solution(mesh):
    placed = (
        P("tensor", "seq"),
        P(None, "seq", "tensor"),
        P("tensor", None),
        P("tensor"),
        P("tensor", "seq"),
    )
    return jax.shard_map(
        per_device, mesh=mesh, in_specs=placed, out_specs=P("seq", "tensor"), check_vma=False
    )
```

```python
import jax
import jax.numpy as jnp
from jax import lax
from jax.sharding import Mesh, PartitionSpec as P


SEQ = ("xlo", "y", "core")
TEN = ("z", "xhi")


def axis_size(names):
    size = 1
    for name in names:
        size *= lax.axis_size(name)
    return size


def from_behind(x, axis, by):
    peers = axis_size(axis)
    pairs = [(i, i + by) for i in range(peers) if 0 <= i + by < peers]
    return lax.ppermute(x, axis, pairs)


def toeplitz_conv(ext, filters):
    groups, taps = filters.shape
    rows, channels = ext.shape
    tok = rows - (taps - 1)
    gw = channels // groups
    nblk = tok // taps
    extp = jnp.concatenate([ext, jnp.zeros((1, channels), ext.dtype)], axis=0)
    blocks = extp.reshape(nblk + 1, taps, groups, gw)
    win = jnp.concatenate([blocks[:-1], blocks[1:]], axis=1)
    w = jnp.pad(filters[:, ::-1], ((0, 0), (0, taps + 1)))
    toe = jnp.tile(w, (1, taps))[:, : taps * 2 * taps].reshape(groups, taps, 2 * taps)
    hi = toe.astype(jnp.bfloat16)
    lo = (toe - hi.astype(jnp.float32)).astype(jnp.bfloat16)
    out = jnp.einsum("gts,isgc->itgc", hi, win, preferred_element_type=jnp.float32)
    out = out + jnp.einsum("gts,isgc->itgc", lo, win, preferred_element_type=jnp.float32)
    return out.reshape(tok, channels)


def per_device(tokens, in_weight, filters, skip_gain, out_weight):
    gathered = lax.all_gather(lax.all_gather(tokens, "xhi", axis=0, tiled=True), "z", axis=0, tiled=True)
    tok_dev = gathered.shape[0] // axis_size(SEQ)
    channels = in_weight.shape[2]
    taps_count = filters.shape[1]
    group_width = channels // filters.shape[0]
    summed = lax.psum_scatter(
        jnp.einsum("rf,sfc->rsc", gathered, in_weight, preferred_element_type=jnp.float32).astype(
            jnp.bfloat16
        ),
        SEQ,
        scatter_dimension=0,
        tiled=True,
    ).astype(jnp.float32)
    query_rows = summed[:, 0].astype(jnp.bfloat16)
    key_rows = summed[:, 1].astype(jnp.bfloat16)
    value_rows = summed[:, 2].astype(jnp.bfloat16)
    product = (key_rows.astype(jnp.float32) * value_rows.astype(jnp.float32)).astype(jnp.bfloat16)
    previous = from_behind(product[tok_dev - (taps_count - 1) :], SEQ, 1)
    product_f = product.astype(jnp.float32)
    extended = jnp.concatenate([previous, product], axis=0)
    conv = toeplitz_conv(extended, filters)
    conv = conv + skip_gain[None, :] * product_f
    gated = (query_rows.astype(jnp.float32) * conv).astype(jnp.bfloat16)
    partial_out = jnp.dot(
        gated,
        lax.all_gather(out_weight, SEQ, axis=1, tiled=True),
        preferred_element_type=jnp.float32,
    )
    rows, cols = partial_out.shape
    n_z, n_x = lax.axis_size("z"), lax.axis_size("xhi")
    split = partial_out.astype(jnp.bfloat16).reshape(rows, n_z, n_x, cols // (n_z * n_x))
    split = lax.psum_scatter(split, "z", scatter_dimension=1, tiled=True)
    split = lax.psum_scatter(split, "xhi", scatter_dimension=2, tiled=True)
    return split.reshape(rows, cols // (n_z * n_x))


def solution(mesh):
    n_seq, n_ten = mesh.devices.shape
    fine = Mesh(mesh.devices.reshape(2, 4, 2, n_ten // 2, 2), SEQ + TEN)
    placed = (
        P(TEN, SEQ),
        P(None, SEQ, TEN),
        P(TEN, None),
        P(TEN),
        P(TEN, SEQ),
    )
    return jax.shard_map(
        per_device, mesh=fine, in_specs=placed, out_specs=P(SEQ, TEN), check_vma=False
    )
```

```python
import jax
import jax.numpy as jnp
from jax import lax
from jax.sharding import Mesh, PartitionSpec as P


SEQ = ("xlo", "y", "core")
TEN = ("z", "xhi")


def axis_size(names):
    size = 1
    for name in names:
        size *= lax.axis_size(name)
    return size


def from_behind(x, axis, by):
    peers = axis_size(axis)
    pairs = [(i, i + by) for i in range(peers) if 0 <= i + by < peers]
    return lax.ppermute(x, axis, pairs)


def toeplitz_conv(ext, filters):
    groups, taps = filters.shape
    rows, channels = ext.shape
    tok = rows - (taps - 1)
    gw = channels // groups
    nblk = tok // taps
    extp = jnp.concatenate([ext, jnp.zeros((1, channels), ext.dtype)], axis=0)
    blocks = extp.reshape(nblk + 1, taps, groups, gw)
    win = jnp.concatenate([blocks[:-1], blocks[1:]], axis=1)
    w = jnp.pad(filters[:, ::-1], ((0, 0), (0, taps + 1)))
    toe = jnp.tile(w, (1, taps))[:, : taps * 2 * taps].reshape(groups, taps, 2 * taps)
    hi = toe.astype(jnp.bfloat16)
    lo = (toe - hi.astype(jnp.float32)).astype(jnp.bfloat16)
    out = jnp.einsum("gts,isgc->itgc", hi, win, preferred_element_type=jnp.float32)
    out = out + jnp.einsum("gts,isgc->itgc", lo, win, preferred_element_type=jnp.float32)
    return out.reshape(tok, channels)


def per_device(tokens, in_weight, filters, skip_gain, out_weight):
    gathered = lax.all_gather(lax.all_gather(tokens, "xhi", axis=0, tiled=True), "z", axis=0, tiled=True)
    tok_dev = gathered.shape[0] // axis_size(SEQ)
    channels = in_weight.shape[2]
    taps_count = filters.shape[1]
    group_width = channels // filters.shape[0]
    summed = lax.psum_scatter(
        jnp.einsum("rf,sfc->rsc", gathered, in_weight, preferred_element_type=jnp.float32).astype(
            jnp.bfloat16
        ),
        SEQ,
        scatter_dimension=0,
        tiled=True,
    ).astype(jnp.float32)
    query_rows = summed[:, 0].astype(jnp.bfloat16)
    key_rows = summed[:, 1].astype(jnp.bfloat16)
    value_rows = summed[:, 2].astype(jnp.bfloat16)
    product = (key_rows.astype(jnp.float32) * value_rows.astype(jnp.float32)).astype(jnp.bfloat16)
    previous = from_behind(product[tok_dev - (taps_count - 1) :], SEQ, 1)
    product_f = product.astype(jnp.float32)
    extended = jnp.concatenate([previous, product], axis=0)
    conv = toeplitz_conv(extended, filters)
    conv = conv + skip_gain[None, :] * product_f
    gated = (query_rows.astype(jnp.float32) * conv).astype(jnp.bfloat16)
    w_chips = lax.all_gather(out_weight, ("xlo", "y"), axis=0, tiled=False)
    w_all = lax.all_gather(w_chips, "core", axis=0, tiled=False)
    partial_out = jnp.einsum(
        "tc,jkco->jkto", gated, jnp.swapaxes(w_all, 0, 1), preferred_element_type=jnp.float32
    ).astype(jnp.bfloat16)
    by_z = lax.psum_scatter(partial_out, "z", scatter_dimension=0, tiled=True)[0]
    me = lax.axis_index("xhi")
    keep = lax.dynamic_index_in_dim(by_z, me, 0, keepdims=False)
    give = lax.dynamic_index_in_dim(by_z, 1 - me, 0, keepdims=False)
    got = lax.ppermute(give, "xhi", [(0, 1), (1, 0)])
    return (keep.astype(jnp.float32) + got.astype(jnp.float32)).astype(jnp.bfloat16)


def solution(mesh):
    n_seq, n_ten = mesh.devices.shape
    fine = Mesh(mesh.devices.reshape(2, 4, 2, n_ten // 2, 2), SEQ + TEN)
    placed = (
        P(TEN, SEQ),
        P(None, SEQ, TEN),
        P(TEN, None),
        P(TEN),
        P(TEN, SEQ),
    )
    return jax.shard_map(
        per_device, mesh=fine, in_specs=placed, out_specs=P(SEQ, TEN), check_vma=False
    )
```

```python
import jax
import jax.numpy as jnp
from jax import lax
from jax.sharding import Mesh, PartitionSpec as P


SEQ = ("xlo", "y", "core")
TEN = ("z", "xhi")


def axis_size(names):
    size = 1
    for name in names:
        size *= lax.axis_size(name)
    return size


def from_behind(x, axis, by):
    peers = axis_size(axis)
    pairs = [(i, i + by) for i in range(peers) if 0 <= i + by < peers]
    return lax.ppermute(x, axis, pairs)


def toeplitz_conv(ext, filters):
    groups, taps = filters.shape
    rows, channels = ext.shape
    tok = rows - (taps - 1)
    gw = channels // groups
    nblk = tok // taps
    extp = jnp.concatenate([ext, jnp.zeros((1, channels), ext.dtype)], axis=0)
    blocks = extp.reshape(nblk + 1, taps, groups, gw)
    win = jnp.concatenate([blocks[:-1], blocks[1:]], axis=1)
    w = jnp.pad(filters[:, ::-1], ((0, 0), (0, taps + 1)))
    toe = jnp.tile(w, (1, taps))[:, : taps * 2 * taps].reshape(groups, taps, 2 * taps)
    hi = toe.astype(jnp.bfloat16)
    lo = (toe - hi.astype(jnp.float32)).astype(jnp.bfloat16)
    out = jnp.einsum("gts,isgc->itgc", hi, win, preferred_element_type=jnp.float32)
    out = out + jnp.einsum("gts,isgc->itgc", lo, win, preferred_element_type=jnp.float32)
    return out.reshape(tok, channels)


def per_device(tokens, in_weight, filters, skip_gain, out_weight):
    gathered = lax.all_gather(lax.all_gather(tokens, "xhi", axis=0, tiled=True), "z", axis=0, tiled=True)
    chips = axis_size(("xlo", "y"))
    spread = jnp.broadcast_to(out_weight[None], (chips,) + out_weight.shape)
    w_mine = lax.all_to_all(spread, ("xlo", "y"), 0, 0, tiled=True)
    gathered, w_mine = lax.optimization_barrier((gathered, w_mine))
    tok_dev = gathered.shape[0] // axis_size(SEQ)
    channels = in_weight.shape[2]
    taps_count = filters.shape[1]
    group_width = channels // filters.shape[0]
    summed = lax.psum_scatter(
        jnp.einsum("rf,sfc->rsc", gathered, in_weight, preferred_element_type=jnp.float32).astype(
            jnp.bfloat16
        ),
        SEQ,
        scatter_dimension=0,
        tiled=True,
    ).astype(jnp.float32)
    query_rows = summed[:, 0].astype(jnp.bfloat16)
    key_rows = summed[:, 1].astype(jnp.bfloat16)
    value_rows = summed[:, 2].astype(jnp.bfloat16)
    product = (key_rows.astype(jnp.float32) * value_rows.astype(jnp.float32)).astype(jnp.bfloat16)
    previous = from_behind(product[tok_dev - (taps_count - 1) :], SEQ, 1)
    product_f = product.astype(jnp.float32)
    extended = jnp.concatenate([previous, product], axis=0)
    conv = toeplitz_conv(extended, filters)
    conv = conv + skip_gain[None, :] * product_f
    gated = (query_rows.astype(jnp.float32) * conv).astype(jnp.bfloat16)
    w_other = lax.ppermute(w_mine, "core", [(0, 1), (1, 0)])
    partial_out = jnp.einsum(
        "tc,jmco->jmto", gated, jnp.stack([w_mine, w_other], axis=1), preferred_element_type=jnp.float32
    ).astype(jnp.bfloat16)
    by_z = lax.psum_scatter(partial_out, "z", scatter_dimension=0, tiled=True)[0]
    keep_at = (lax.axis_index("xhi") != lax.axis_index("core")).astype(jnp.int32)
    keep = lax.dynamic_index_in_dim(by_z, keep_at, 0, keepdims=False)
    give = lax.dynamic_index_in_dim(by_z, 1 - keep_at, 0, keepdims=False)
    got = lax.ppermute(give, "xhi", [(0, 1), (1, 0)])
    return (keep.astype(jnp.float32) + got.astype(jnp.float32)).astype(jnp.bfloat16)


def solution(mesh):
    n_seq, n_ten = mesh.devices.shape
    fine = Mesh(mesh.devices.reshape(2, 4, 2, n_ten // 2, 2), SEQ + TEN)
    placed = (
        P(TEN, SEQ),
        P(None, SEQ, TEN),
        P(TEN, None),
        P(TEN),
        P(TEN, SEQ),
    )
    return jax.shard_map(
        per_device, mesh=fine, in_specs=placed, out_specs=P(SEQ, TEN), check_vma=False
    )
```

```python
import jax
import jax.numpy as jnp
from jax import lax
from jax.sharding import Mesh, PartitionSpec as P


SEQ = ("xlo", "y", "core")
TEN = ("z", "xhi")


def axis_size(names):
    size = 1
    for name in names:
        size *= lax.axis_size(name)
    return size


def from_behind(x, axis, by):
    peers = axis_size(axis)
    pairs = [(i, i + by) for i in range(peers) if 0 <= i + by < peers]
    return lax.ppermute(x, axis, pairs)


def toeplitz_conv(ext, filters):
    groups, taps = filters.shape
    rows, channels = ext.shape
    tok = rows - (taps - 1)
    gw = channels // groups
    nblk = tok // taps
    extp = jnp.concatenate([ext, jnp.zeros((1, channels), ext.dtype)], axis=0)
    blocks = extp.reshape(nblk + 1, taps, groups, gw)
    win = jnp.concatenate([blocks[:-1], blocks[1:]], axis=1)
    w = jnp.pad(filters[:, ::-1], ((0, 0), (0, taps + 1)))
    toe = jnp.tile(w, (1, taps))[:, : taps * 2 * taps].reshape(groups, taps, 2 * taps)
    hi = toe.astype(jnp.bfloat16)
    lo = (toe - hi.astype(jnp.float32)).astype(jnp.bfloat16)
    out = jnp.einsum("gts,isgc->itgc", hi, win, preferred_element_type=jnp.float32)
    out = out + jnp.einsum("gts,isgc->itgc", lo, win, preferred_element_type=jnp.float32)
    return out.reshape(tok, channels)


def per_device(tokens, in_weight, filters, skip_gain, out_weight):
    gathered = lax.all_gather(lax.all_gather(tokens, "xhi", axis=0, tiled=True), "z", axis=0, tiled=True)
    chips = axis_size(("xlo", "y"))
    spread = jnp.broadcast_to(out_weight[None], (chips,) + out_weight.shape)
    w_mine = lax.all_to_all(spread, ("xlo", "y"), 0, 0, tiled=True)
    gathered, w_mine = lax.optimization_barrier((gathered, w_mine))
    tok_dev = gathered.shape[0] // axis_size(SEQ)
    channels = in_weight.shape[2]
    taps_count = filters.shape[1]
    group_width = channels // filters.shape[0]
    kv_part = jnp.einsum(
        "rf,sfc->rsc", gathered, in_weight[1:], preferred_element_type=jnp.float32
    ).astype(jnp.bfloat16)
    kv = lax.psum_scatter(kv_part, SEQ, scatter_dimension=0, tiled=True)
    q_part = jnp.dot(gathered, in_weight[0], preferred_element_type=jnp.float32).astype(jnp.bfloat16)
    q_part, kv = lax.optimization_barrier((q_part, kv))
    query_rows = lax.psum_scatter(q_part, SEQ, scatter_dimension=0, tiled=True)
    key_rows = kv[:, 0]
    value_rows = kv[:, 1]
    product = (key_rows.astype(jnp.float32) * value_rows.astype(jnp.float32)).astype(jnp.bfloat16)
    previous = from_behind(product[tok_dev - (taps_count - 1) :], SEQ, 1)
    product_f = product.astype(jnp.float32)
    extended = jnp.concatenate([previous, product], axis=0)
    conv = toeplitz_conv(extended, filters)
    conv = conv + skip_gain[None, :] * product_f
    gated = (query_rows.astype(jnp.float32) * conv).astype(jnp.bfloat16)
    w_other = lax.ppermute(w_mine, "core", [(0, 1), (1, 0)])
    keep_at = (lax.axis_index("xhi") != lax.axis_index("core")).astype(jnp.int32)
    w_keep = jnp.where(keep_at == 0, w_mine, w_other)
    w_give = jnp.where(keep_at == 0, w_other, w_mine)
    give_part = jnp.einsum("tc,jco->jto", gated, w_give, preferred_element_type=jnp.float32)
    give = lax.psum_scatter(give_part.astype(jnp.bfloat16), "z", scatter_dimension=0, tiled=True)[0]
    keep_part = jnp.einsum("tc,jco->jto", gated, w_keep, preferred_element_type=jnp.float32)
    keep_part, give = lax.optimization_barrier((keep_part.astype(jnp.bfloat16), give))
    got = lax.ppermute(give, "xhi", [(0, 1), (1, 0)])
    keep = lax.psum_scatter(keep_part, "z", scatter_dimension=0, tiled=True)[0]
    return (keep.astype(jnp.float32) + got.astype(jnp.float32)).astype(jnp.bfloat16)


def solution(mesh):
    n_seq, n_ten = mesh.devices.shape
    fine = Mesh(mesh.devices.reshape(2, 4, 2, n_ten // 2, 2), SEQ + TEN)
    placed = (
        P(TEN, SEQ),
        P(None, SEQ, TEN),
        P(TEN, None),
        P(TEN),
        P(TEN, SEQ),
    )
    return jax.shard_map(
        per_device, mesh=fine, in_specs=placed, out_specs=P(SEQ, TEN), check_vma=False
    )
```

```python
import jax
import jax.numpy as jnp
from jax import lax
from jax.sharding import Mesh, PartitionSpec as P


SEQ = ("xlo", "y", "core")
TEN = ("z", "xhi")


def axis_size(names):
    size = 1
    for name in names:
        size *= lax.axis_size(name)
    return size


def from_behind(x, axis, by):
    peers = axis_size(axis)
    pairs = [(i, i + by) for i in range(peers) if 0 <= i + by < peers]
    return lax.ppermute(x, axis, pairs)


def toeplitz_conv(ext, filters):
    groups, taps = filters.shape
    rows, channels = ext.shape
    tok = rows - (taps - 1)
    gw = channels // groups
    nblk = tok // taps
    extp = jnp.concatenate([ext, jnp.zeros((1, channels), ext.dtype)], axis=0)
    blocks = extp.reshape(nblk + 1, taps, groups, gw)
    win = jnp.concatenate([blocks[:-1], blocks[1:]], axis=1)
    w = jnp.pad(filters[:, ::-1], ((0, 0), (0, taps + 1)))
    toe = jnp.tile(w, (1, taps))[:, : taps * 2 * taps].reshape(groups, taps, 2 * taps)
    hi = toe.astype(jnp.bfloat16)
    lo = (toe - hi.astype(jnp.float32)).astype(jnp.bfloat16)
    both = jnp.concatenate([hi, lo], axis=2)
    twice = jnp.concatenate([win, win], axis=1)
    out = jnp.einsum("gts,isgc->itgc", both, twice, preferred_element_type=jnp.float32)
    return out.reshape(tok, channels)


def per_device(tokens, in_weight, filters, skip_gain, out_weight):
    gathered = lax.all_gather(lax.all_gather(tokens, "xhi", axis=0, tiled=True), "z", axis=0, tiled=True)
    chips = axis_size(("xlo", "y"))
    spread = jnp.broadcast_to(out_weight[None], (chips,) + out_weight.shape)
    w_mine = lax.all_to_all(spread, ("xlo", "y"), 0, 0, tiled=True)
    gathered, w_mine = lax.optimization_barrier((gathered, w_mine))
    tok_dev = gathered.shape[0] // axis_size(SEQ)
    channels = in_weight.shape[2]
    taps_count = filters.shape[1]
    group_width = channels // filters.shape[0]
    summed = lax.psum_scatter(
        jnp.einsum("rf,sfc->rsc", gathered, in_weight, preferred_element_type=jnp.float32).astype(
            jnp.bfloat16
        ),
        SEQ,
        scatter_dimension=0,
        tiled=True,
    ).astype(jnp.float32)
    query_rows = summed[:, 0].astype(jnp.bfloat16)
    key_rows = summed[:, 1].astype(jnp.bfloat16)
    value_rows = summed[:, 2].astype(jnp.bfloat16)
    product = (key_rows.astype(jnp.float32) * value_rows.astype(jnp.float32)).astype(jnp.bfloat16)
    previous = from_behind(product[tok_dev - (taps_count - 1) :], SEQ, 1)
    product_f = product.astype(jnp.float32)
    extended = jnp.concatenate([previous, product], axis=0)
    conv = toeplitz_conv(extended, filters)
    conv = conv + skip_gain[None, :] * product_f
    gated = (query_rows.astype(jnp.float32) * conv).astype(jnp.bfloat16)
    w_other = lax.ppermute(w_mine, "core", [(0, 1), (1, 0)])
    partial_out = jnp.einsum(
        "tc,jmco->jmto", gated, jnp.stack([w_mine, w_other], axis=1), preferred_element_type=jnp.float32
    ).astype(jnp.bfloat16)
    by_z = lax.psum_scatter(partial_out, "z", scatter_dimension=0, tiled=True)[0]
    keep_at = (lax.axis_index("xhi") != lax.axis_index("core")).astype(jnp.int32)
    keep = lax.dynamic_index_in_dim(by_z, keep_at, 0, keepdims=False)
    give = lax.dynamic_index_in_dim(by_z, 1 - keep_at, 0, keepdims=False)
    got = lax.ppermute(give, "xhi", [(0, 1), (1, 0)])
    return (keep.astype(jnp.float32) + got.astype(jnp.float32)).astype(jnp.bfloat16)


def solution(mesh):
    n_seq, n_ten = mesh.devices.shape
    fine = Mesh(mesh.devices.reshape(2, 4, 2, n_ten // 2, 2), SEQ + TEN)
    placed = (
        P(TEN, SEQ),
        P(None, SEQ, TEN),
        P(TEN, None),
        P(TEN),
        P(TEN, SEQ),
    )
    return jax.shard_map(
        per_device, mesh=fine, in_specs=placed, out_specs=P(SEQ, TEN), check_vma=False
    )
```

```python
import jax
import jax.numpy as jnp
from jax import lax
from jax.experimental import pallas as pl
from jax.experimental.pallas import tpu as pltpu
from jax.sharding import Mesh, PartitionSpec as P


SEQ = ("xlo", "y", "core")
TEN = ("z", "xhi")


def axis_size(names):
    size = 1
    for name in names:
        size *= lax.axis_size(name)
    return size


def from_behind(x, axis, by):
    peers = axis_size(axis)
    pairs = [(i, i + by) for i in range(peers) if 0 <= i + by < peers]
    return lax.ppermute(x, axis, pairs)


def toeplitz_conv(ext, filters):
    groups, taps = filters.shape
    rows, channels = ext.shape
    tok = rows - (taps - 1)
    gw = channels // groups
    nblk = tok // taps
    extp = jnp.concatenate([ext, jnp.zeros((1, channels), ext.dtype)], axis=0)
    blocks = extp.reshape(nblk + 1, taps, groups, gw)
    win = jnp.concatenate([blocks[:-1], blocks[1:]], axis=1)
    w = jnp.pad(filters[:, ::-1], ((0, 0), (0, taps + 1)))
    toe = jnp.tile(w, (1, taps))[:, : taps * 2 * taps].reshape(groups, taps, 2 * taps)
    hi = toe.astype(jnp.bfloat16)
    lo = (toe - hi.astype(jnp.float32)).astype(jnp.bfloat16)
    both = jnp.concatenate([hi, lo], axis=2)
    twice = jnp.concatenate([win, win], axis=1)
    out = jnp.einsum("gts,isgc->itgc", both, twice, preferred_element_type=jnp.float32)
    return out.reshape(tok, channels)


def out_proj_kernel(g_ref, wm_ref, wo_ref, out_ref):
    g = g_ref[...]
    for jj in range(wm_ref.shape[0]):
        out_ref[jj, 0] = jnp.dot(g, wm_ref[jj], preferred_element_type=jnp.float32).astype(out_ref.dtype)
        out_ref[jj, 1] = jnp.dot(g, wo_ref[jj], preferred_element_type=jnp.float32).astype(out_ref.dtype)


def out_proj(gated, w_mine, w_other, per_step=2):
    rows, depth = gated.shape
    blocks, _, width = w_mine.shape
    w_spec = pl.BlockSpec((per_step, depth, width), lambda i: (i, 0, 0))
    return pl.pallas_call(
        out_proj_kernel,
        out_shape=jax.ShapeDtypeStruct((blocks, 2, rows, width), jnp.bfloat16),
        grid=(blocks // per_step,),
        in_specs=[pl.BlockSpec((rows, depth), lambda i: (0, 0)), w_spec, w_spec],
        out_specs=pl.BlockSpec((per_step, 2, rows, width), lambda i: (i, 0, 0, 0)),
        cost_estimate=pl.CostEstimate(
            flops=2 * rows * depth * width * blocks * 2,
            bytes_accessed=2 * (rows * depth + 2 * blocks * depth * width + 2 * blocks * rows * width),
            transcendentals=0,
        ),
    )(gated, w_mine, w_other)


def per_device(tokens, in_weight, filters, skip_gain, out_weight):
    gathered = lax.all_gather(lax.all_gather(tokens, "xhi", axis=0, tiled=True), "z", axis=0, tiled=True)
    chips = axis_size(("xlo", "y"))
    spread = jnp.broadcast_to(out_weight[None], (chips,) + out_weight.shape)
    w_mine = lax.all_to_all(spread, ("xlo", "y"), 0, 0, tiled=True)
    gathered, w_mine = lax.optimization_barrier((gathered, w_mine))
    tok_dev = gathered.shape[0] // axis_size(SEQ)
    channels = in_weight.shape[2]
    taps_count = filters.shape[1]
    group_width = channels // filters.shape[0]
    summed = lax.psum_scatter(
        jnp.einsum("rf,sfc->rsc", gathered, in_weight, preferred_element_type=jnp.float32).astype(
            jnp.bfloat16
        ),
        SEQ,
        scatter_dimension=0,
        tiled=True,
    ).astype(jnp.float32)
    query_rows = summed[:, 0].astype(jnp.bfloat16)
    key_rows = summed[:, 1].astype(jnp.bfloat16)
    value_rows = summed[:, 2].astype(jnp.bfloat16)
    product = (key_rows.astype(jnp.float32) * value_rows.astype(jnp.float32)).astype(jnp.bfloat16)
    previous = from_behind(product[tok_dev - (taps_count - 1) :], SEQ, 1)
    product_f = product.astype(jnp.float32)
    extended = jnp.concatenate([previous, product], axis=0)
    conv = toeplitz_conv(extended, filters)
    conv = conv + skip_gain[None, :] * product_f
    gated = (query_rows.astype(jnp.float32) * conv).astype(jnp.bfloat16)
    w_other = lax.ppermute(w_mine, "core", [(0, 1), (1, 0)])
    partial_out = out_proj(gated, w_mine, w_other)
    by_z = lax.psum_scatter(partial_out, "z", scatter_dimension=0, tiled=True)[0]
    keep_at = (lax.axis_index("xhi") != lax.axis_index("core")).astype(jnp.int32)
    keep = lax.dynamic_index_in_dim(by_z, keep_at, 0, keepdims=False)
    give = lax.dynamic_index_in_dim(by_z, 1 - keep_at, 0, keepdims=False)
    got = lax.ppermute(give, "xhi", [(0, 1), (1, 0)])
    return (keep.astype(jnp.float32) + got.astype(jnp.float32)).astype(jnp.bfloat16)


def solution(mesh):
    n_seq, n_ten = mesh.devices.shape
    fine = Mesh(mesh.devices.reshape(2, 4, 2, n_ten // 2, 2), SEQ + TEN)
    placed = (
        P(TEN, SEQ),
        P(None, SEQ, TEN),
        P(TEN, None),
        P(TEN),
        P(TEN, SEQ),
    )
    return jax.shard_map(
        per_device, mesh=fine, in_specs=placed, out_specs=P(SEQ, TEN), check_vma=False
    )
```

```python
import jax
import jax.numpy as jnp
from jax import lax
from jax.experimental import pallas as pl
from jax.experimental.pallas import tpu as pltpu
from jax.sharding import Mesh, PartitionSpec as P


SEQ = ("xlo", "y", "core")
TEN = ("z", "xhi")


def axis_size(names):
    size = 1
    for name in names:
        size *= lax.axis_size(name)
    return size


def from_behind(x, axis, by):
    peers = axis_size(axis)
    pairs = [(i, i + by) for i in range(peers) if 0 <= i + by < peers]
    return lax.ppermute(x, axis, pairs)


def toeplitz_conv(ext, filters):
    groups, taps = filters.shape
    rows, channels = ext.shape
    tok = rows - (taps - 1)
    gw = channels // groups
    nblk = tok // taps
    extp = jnp.concatenate([ext, jnp.zeros((1, channels), ext.dtype)], axis=0)
    blocks = extp.reshape(nblk + 1, taps, groups, gw)
    win = jnp.concatenate([blocks[:-1], blocks[1:]], axis=1)
    w = jnp.pad(filters[:, ::-1], ((0, 0), (0, taps + 1)))
    toe = jnp.tile(w, (1, taps))[:, : taps * 2 * taps].reshape(groups, taps, 2 * taps)
    hi = toe.astype(jnp.bfloat16)
    lo = (toe - hi.astype(jnp.float32)).astype(jnp.bfloat16)
    both = jnp.concatenate([hi, lo], axis=2)
    twice = jnp.concatenate([win, win], axis=1)
    out = jnp.einsum("gts,isgc->itgc", both, twice, preferred_element_type=jnp.float32)
    return out.reshape(tok, channels)


def out_proj_kernel(gt_ref, wm_ref, wo_ref, out_ref):
    gt = gt_ref[...]
    step, width, depth = wm_ref.shape
    for m, w_ref in enumerate((wm_ref, wo_ref)):
        res = jnp.dot(w_ref[...].reshape(step * width, depth), gt, preferred_element_type=jnp.float32)
        res = res.astype(out_ref.dtype).reshape(step, width, gt.shape[1])
        for jj in range(step):
            out_ref[jj, m] = res[jj]


def out_proj(gated_t, wt_mine, wt_other, per_step=4):
    depth, rows = gated_t.shape
    blocks, width, _ = wt_mine.shape
    w_spec = pl.BlockSpec((per_step, width, depth), lambda i: (i, 0, 0))
    return pl.pallas_call(
        out_proj_kernel,
        out_shape=jax.ShapeDtypeStruct((blocks, 2, width, rows), jnp.bfloat16),
        grid=(blocks // per_step,),
        in_specs=[pl.BlockSpec((depth, rows), lambda i: (0, 0)), w_spec, w_spec],
        out_specs=pl.BlockSpec((per_step, 2, width, rows), lambda i: (i, 0, 0, 0)),
        cost_estimate=pl.CostEstimate(
            flops=2 * rows * depth * width * blocks * 2,
            bytes_accessed=2 * (rows * depth + 2 * blocks * depth * width + 2 * blocks * rows * width),
            transcendentals=0,
        ),
    )(gated_t, wt_mine, wt_other)


def per_device(tokens, in_weight, filters, skip_gain, out_weight):
    gathered = lax.all_gather(lax.all_gather(tokens, "xhi", axis=0, tiled=True), "z", axis=0, tiled=True)
    chips = axis_size(("xlo", "y"))
    spread = jnp.broadcast_to(out_weight[None], (chips,) + out_weight.shape)
    w_mine = lax.all_to_all(spread, ("xlo", "y"), 0, 0, tiled=True)
    gathered, w_mine = lax.optimization_barrier((gathered, w_mine))
    tok_dev = gathered.shape[0] // axis_size(SEQ)
    channels = in_weight.shape[2]
    taps_count = filters.shape[1]
    group_width = channels // filters.shape[0]
    summed = lax.psum_scatter(
        jnp.einsum("rf,sfc->rsc", gathered, in_weight, preferred_element_type=jnp.float32).astype(
            jnp.bfloat16
        ),
        SEQ,
        scatter_dimension=0,
        tiled=True,
    ).astype(jnp.float32)
    query_rows = summed[:, 0].astype(jnp.bfloat16)
    key_rows = summed[:, 1].astype(jnp.bfloat16)
    value_rows = summed[:, 2].astype(jnp.bfloat16)
    product = (key_rows.astype(jnp.float32) * value_rows.astype(jnp.float32)).astype(jnp.bfloat16)
    previous = from_behind(product[tok_dev - (taps_count - 1) :], SEQ, 1)
    product_f = product.astype(jnp.float32)
    extended = jnp.concatenate([previous, product], axis=0)
    conv = toeplitz_conv(extended, filters)
    conv = conv + skip_gain[None, :] * product_f
    gated = (query_rows.astype(jnp.float32) * conv).astype(jnp.bfloat16)
    w_other = lax.ppermute(w_mine, "core", [(0, 1), (1, 0)])
    partial_out = out_proj(gated.T, jnp.swapaxes(w_mine, 1, 2), jnp.swapaxes(w_other, 1, 2))
    by_z = lax.psum_scatter(partial_out, "z", scatter_dimension=0, tiled=True)[0]
    keep_at = (lax.axis_index("xhi") != lax.axis_index("core")).astype(jnp.int32)
    keep = lax.dynamic_index_in_dim(by_z, keep_at, 0, keepdims=False)
    give = lax.dynamic_index_in_dim(by_z, 1 - keep_at, 0, keepdims=False)
    got = lax.ppermute(give, "xhi", [(0, 1), (1, 0)])
    return (keep.astype(jnp.float32) + got.astype(jnp.float32)).astype(jnp.bfloat16).T


def solution(mesh):
    n_seq, n_ten = mesh.devices.shape
    fine = Mesh(mesh.devices.reshape(2, 4, 2, n_ten // 2, 2), SEQ + TEN)
    placed = (
        P(TEN, SEQ),
        P(None, SEQ, TEN),
        P(TEN, None),
        P(TEN),
        P(TEN, SEQ),
    )
    return jax.shard_map(
        per_device, mesh=fine, in_specs=placed, out_specs=P(SEQ, TEN), check_vma=False
    )
```

```python
import jax
import jax.numpy as jnp
from jax import lax
from jax.experimental import pallas as pl
from jax.experimental.pallas import tpu as pltpu
from jax.sharding import Mesh, PartitionSpec as P


SEQ = ("xlo", "y", "core")
TEN = ("z", "xhi")


def axis_size(names):
    size = 1
    for name in names:
        size *= lax.axis_size(name)
    return size


def from_behind(x, axis, by):
    peers = axis_size(axis)
    pairs = [(i, i + by) for i in range(peers) if 0 <= i + by < peers]
    return lax.ppermute(x, axis, pairs)


def toeplitz_conv(ext, filters):
    groups, taps = filters.shape
    rows, channels = ext.shape
    tok = rows - (taps - 1)
    gw = channels // groups
    nblk = tok // taps
    extp = jnp.concatenate([ext, jnp.zeros((1, channels), ext.dtype)], axis=0)
    blocks = extp.reshape(nblk + 1, taps, groups, gw)
    win = jnp.concatenate([blocks[:-1], blocks[1:]], axis=1)
    w = jnp.pad(filters[:, ::-1], ((0, 0), (0, taps + 1)))
    toe = jnp.tile(w, (1, taps))[:, : taps * 2 * taps].reshape(groups, taps, 2 * taps)
    hi = toe.astype(jnp.bfloat16)
    lo = (toe - hi.astype(jnp.float32)).astype(jnp.bfloat16)
    both = jnp.concatenate([hi, lo], axis=2)
    twice = jnp.concatenate([win, win], axis=1)
    out = jnp.einsum("gts,isgc->itgc", both, twice, preferred_element_type=jnp.float32)
    return out.reshape(tok, channels)


def out_proj_kernel(gt_ref, w_ref, *rest):
    out_ref = rest[-1]
    step, width, depth = w_ref.shape
    res = jnp.dot(w_ref[...].reshape(step * width, depth), gt_ref[...], preferred_element_type=jnp.float32)
    res = res.reshape(step, width, gt_ref.shape[1])
    if len(rest) == 2:
        res = res + rest[0][...].astype(jnp.float32)
    out_ref[...] = res.astype(out_ref.dtype)


def out_proj(gated_t, weight_t, acc=None, per_step=4):
    depth, rows = gated_t.shape
    blocks, width, _ = weight_t.shape
    block = pl.BlockSpec((per_step, width, rows), lambda i: (i, 0, 0))
    specs = [pl.BlockSpec((depth, rows), lambda i: (0, 0)), pl.BlockSpec((per_step, width, depth), lambda i: (i, 0, 0))]
    operands = [gated_t, weight_t]
    if acc is not None:
        specs.append(block)
        operands.append(acc)
    return pl.pallas_call(
        out_proj_kernel,
        out_shape=jax.ShapeDtypeStruct((blocks, width, rows), jnp.bfloat16),
        grid=(blocks // per_step,),
        in_specs=specs,
        out_specs=block,
        cost_estimate=pl.CostEstimate(
            flops=2 * rows * depth * width * blocks,
            bytes_accessed=2 * (rows * depth + blocks * depth * width + len(operands) * blocks * rows * width),
            transcendentals=0,
        ),
    )(*operands)


def per_device(tokens, in_weight, filters, skip_gain, out_weight):
    gathered = lax.all_gather(lax.all_gather(tokens, "xhi", axis=0, tiled=True), "z", axis=0, tiled=True)
    chips = axis_size(("xlo", "y"))
    spread = jnp.broadcast_to(out_weight[None], (chips,) + out_weight.shape)
    w_mine = lax.all_to_all(spread, ("xlo", "y"), 0, 0, tiled=True)
    gathered, w_mine = lax.optimization_barrier((gathered, w_mine))
    tok_dev = gathered.shape[0] // axis_size(SEQ)
    channels = in_weight.shape[2]
    taps_count = filters.shape[1]
    group_width = channels // filters.shape[0]
    summed = lax.psum_scatter(
        jnp.einsum("rf,sfc->rsc", gathered, in_weight, preferred_element_type=jnp.float32).astype(
            jnp.bfloat16
        ),
        SEQ,
        scatter_dimension=0,
        tiled=True,
    ).astype(jnp.float32)
    query_rows = summed[:, 0].astype(jnp.bfloat16)
    key_rows = summed[:, 1].astype(jnp.bfloat16)
    value_rows = summed[:, 2].astype(jnp.bfloat16)
    product = (key_rows.astype(jnp.float32) * value_rows.astype(jnp.float32)).astype(jnp.bfloat16)
    previous = from_behind(product[tok_dev - (taps_count - 1) :], SEQ, 1)
    product_f = product.astype(jnp.float32)
    extended = jnp.concatenate([previous, product], axis=0)
    conv = toeplitz_conv(extended, filters)
    conv = conv + skip_gain[None, :] * product_f
    gated = (query_rows.astype(jnp.float32) * conv).astype(jnp.bfloat16)
    w_other = lax.ppermute(w_mine, "core", [(0, 1), (1, 0)])
    swap = [(0, 1), (1, 0)]
    same = lax.axis_index("xhi") == lax.axis_index("core")
    keep_w = jnp.where(same, w_mine, w_other)
    give_w = jnp.where(same, w_other, w_mine)
    recv_w = lax.ppermute(give_w, "xhi", swap)
    recv_g = lax.ppermute(gated, "xhi", swap)
    mine = out_proj(gated.T, jnp.swapaxes(keep_w, 1, 2))
    both = out_proj(recv_g.T, jnp.swapaxes(recv_w, 1, 2), mine)
    summed = lax.psum_scatter(both, "z", scatter_dimension=0, tiled=True)[0]
    return summed.T


def solution(mesh):
    n_seq, n_ten = mesh.devices.shape
    fine = Mesh(mesh.devices.reshape(2, 4, 2, n_ten // 2, 2), SEQ + TEN)
    placed = (
        P(TEN, SEQ),
        P(None, SEQ, TEN),
        P(TEN, None),
        P(TEN),
        P(TEN, SEQ),
    )
    return jax.shard_map(
        per_device, mesh=fine, in_specs=placed, out_specs=P(SEQ, TEN), check_vma=False
    )
```

```python
import jax
import jax.numpy as jnp
from jax import lax
from jax.experimental import pallas as pl
from jax.experimental.pallas import tpu as pltpu
from jax.sharding import Mesh, PartitionSpec as P


SEQ = ("xlo", "y", "core")
TEN = ("z", "xhi")


def axis_size(names):
    size = 1
    for name in names:
        size *= lax.axis_size(name)
    return size


def from_behind(x, axis, by):
    peers = axis_size(axis)
    pairs = [(i, i + by) for i in range(peers) if 0 <= i + by < peers]
    return lax.ppermute(x, axis, pairs)


def toeplitz_conv(ext, filters):
    groups, taps = filters.shape
    rows, channels = ext.shape
    tok = rows - (taps - 1)
    gw = channels // groups
    nblk = tok // taps
    extp = jnp.concatenate([ext, jnp.zeros((1, channels), ext.dtype)], axis=0)
    blocks = extp.reshape(nblk + 1, taps, groups, gw)
    win = jnp.concatenate([blocks[:-1], blocks[1:]], axis=1)
    w = jnp.pad(filters[:, ::-1], ((0, 0), (0, taps + 1)))
    toe = jnp.tile(w, (1, taps))[:, : taps * 2 * taps].reshape(groups, taps, 2 * taps)
    hi = toe.astype(jnp.bfloat16)
    lo = (toe - hi.astype(jnp.float32)).astype(jnp.bfloat16)
    both = jnp.concatenate([hi, lo], axis=2)
    twice = jnp.concatenate([win, win], axis=1)
    out = jnp.einsum("gts,isgc->itgc", both, twice, preferred_element_type=jnp.float32)
    return out.reshape(tok, channels)


def out_proj_kernel(gt_ref, w_ref, *rest):
    out_ref = rest[-1]
    step, width, depth = w_ref.shape
    res = jnp.dot(w_ref[...].reshape(step * width, depth), gt_ref[...], preferred_element_type=jnp.float32)
    res = res.reshape(step, width, gt_ref.shape[1])
    if len(rest) == 2:
        res = res + rest[0][...].astype(jnp.float32)
    out_ref[...] = res.astype(out_ref.dtype)


def out_proj(gated_t, weight_t, acc=None, per_step=4):
    depth, rows = gated_t.shape
    blocks, width, _ = weight_t.shape
    block = pl.BlockSpec((per_step, width, rows), lambda i: (i, 0, 0))
    specs = [pl.BlockSpec((depth, rows), lambda i: (0, 0)), pl.BlockSpec((per_step, width, depth), lambda i: (i, 0, 0))]
    operands = [gated_t, weight_t]
    if acc is not None:
        specs.append(block)
        operands.append(acc)
    return pl.pallas_call(
        out_proj_kernel,
        out_shape=jax.ShapeDtypeStruct((blocks, width, rows), jnp.bfloat16),
        grid=(blocks // per_step,),
        in_specs=specs,
        out_specs=block,
        cost_estimate=pl.CostEstimate(
            flops=2 * rows * depth * width * blocks,
            bytes_accessed=2 * (rows * depth + blocks * depth * width + len(operands) * blocks * rows * width),
            transcendentals=0,
        ),
    )(*operands)


def per_device(tokens, in_weight, filters, skip_gain, out_weight):
    gathered = lax.all_gather(lax.all_gather(tokens, "xhi", axis=0, tiled=True), "z", axis=0, tiled=True)
    swap = [(0, 1), (1, 0)]
    same = lax.axis_index("xhi") == lax.axis_index("core")
    across = lax.ppermute(lax.ppermute(out_weight, "xhi", swap), "core", swap)
    chunk = jnp.where(same, out_weight, across)
    chips = axis_size(("xlo", "y"))
    spread = jnp.broadcast_to(chunk[None], (chips,) + chunk.shape)
    plane = lax.all_to_all(spread, ("xlo", "y"), 0, 0, tiled=True)
    gathered, plane = lax.optimization_barrier((gathered, plane))
    tok_dev = gathered.shape[0] // axis_size(SEQ)
    channels = in_weight.shape[2]
    taps_count = filters.shape[1]
    group_width = channels // filters.shape[0]
    summed = lax.psum_scatter(
        jnp.einsum("rf,sfc->rsc", gathered, in_weight, preferred_element_type=jnp.float32).astype(
            jnp.bfloat16
        ),
        SEQ,
        scatter_dimension=0,
        tiled=True,
    ).astype(jnp.float32)
    query_rows = summed[:, 0].astype(jnp.bfloat16)
    key_rows = summed[:, 1].astype(jnp.bfloat16)
    value_rows = summed[:, 2].astype(jnp.bfloat16)
    product = (key_rows.astype(jnp.float32) * value_rows.astype(jnp.float32)).astype(jnp.bfloat16)
    previous = from_behind(product[tok_dev - (taps_count - 1) :], SEQ, 1)
    product_f = product.astype(jnp.float32)
    extended = jnp.concatenate([previous, product], axis=0)
    conv = toeplitz_conv(extended, filters)
    conv = conv + skip_gain[None, :] * product_f
    gated = (query_rows.astype(jnp.float32) * conv).astype(jnp.bfloat16)
    plane_other = lax.ppermute(plane, "core", swap)
    keep_w = jnp.where(same, plane, plane_other)
    recv_w = jnp.where(same, plane_other, plane)
    recv_g = lax.ppermute(gated, "xhi", swap)
    mine = out_proj(gated.T, jnp.swapaxes(keep_w, 1, 2))
    both = out_proj(recv_g.T, jnp.swapaxes(recv_w, 1, 2), mine)
    summed = lax.psum_scatter(both, "z", scatter_dimension=0, tiled=True)[0]
    return summed.T


def solution(mesh):
    n_seq, n_ten = mesh.devices.shape
    fine = Mesh(mesh.devices.reshape(2, 4, 2, n_ten // 2, 2), SEQ + TEN)
    placed = (
        P(TEN, SEQ),
        P(None, SEQ, TEN),
        P(TEN, None),
        P(TEN),
        P(TEN, SEQ),
    )
    return jax.shard_map(
        per_device, mesh=fine, in_specs=placed, out_specs=P(SEQ, TEN), check_vma=False
    )
```

```python
import jax
import jax.numpy as jnp
from jax import lax
from jax.experimental import pallas as pl
from jax.experimental.pallas import tpu as pltpu
from jax.sharding import Mesh, PartitionSpec as P


SEQ = ("xlo", "y", "core")
TEN = ("z", "xhi")


def axis_size(names):
    size = 1
    for name in names:
        size *= lax.axis_size(name)
    return size


def from_behind(x, axis, by):
    peers = axis_size(axis)
    pairs = [(i, i + by) for i in range(peers) if 0 <= i + by < peers]
    return lax.ppermute(x, axis, pairs)


def toeplitz_conv(ext, filters):
    groups, taps = filters.shape
    rows, channels = ext.shape
    tok = rows - (taps - 1)
    gw = channels // groups
    nblk = tok // taps
    extp = jnp.concatenate([ext, jnp.zeros((1, channels), ext.dtype)], axis=0)
    blocks = extp.reshape(nblk + 1, taps, groups, gw)
    win = jnp.concatenate([blocks[:-1], blocks[1:]], axis=1)
    w = jnp.pad(filters[:, ::-1], ((0, 0), (0, taps + 1)))
    toe = jnp.tile(w, (1, taps))[:, : taps * 2 * taps].reshape(groups, taps, 2 * taps)
    hi = toe.astype(jnp.bfloat16)
    lo = (toe - hi.astype(jnp.float32)).astype(jnp.bfloat16)
    both = jnp.concatenate([hi, lo], axis=2)
    twice = jnp.concatenate([win, win], axis=1)
    out = jnp.einsum("gts,isgc->itgc", both, twice, preferred_element_type=jnp.float32)
    return out.reshape(tok, channels)


def out_proj_kernel(gt_ref, w_ref, *rest):
    out_ref = rest[-1]
    step, width, depth = w_ref.shape
    res = jnp.dot(w_ref[...].reshape(step * width, depth), gt_ref[...], preferred_element_type=jnp.float32)
    res = res.reshape(step, width, gt_ref.shape[1])
    if len(rest) == 2:
        res = res + rest[0][...].astype(jnp.float32)
    out_ref[...] = res.astype(out_ref.dtype)


def out_proj(gated_t, weight_t, acc=None, per_step=4):
    depth, rows = gated_t.shape
    blocks, width, _ = weight_t.shape
    block = pl.BlockSpec((per_step, width, rows), lambda i: (i, 0, 0))
    specs = [pl.BlockSpec((depth, rows), lambda i: (0, 0)), pl.BlockSpec((per_step, width, depth), lambda i: (i, 0, 0))]
    operands = [gated_t, weight_t]
    if acc is not None:
        specs.append(block)
        operands.append(acc)
    return pl.pallas_call(
        out_proj_kernel,
        out_shape=jax.ShapeDtypeStruct((blocks, width, rows), jnp.bfloat16),
        grid=(blocks // per_step,),
        in_specs=specs,
        out_specs=block,
        cost_estimate=pl.CostEstimate(
            flops=2 * rows * depth * width * blocks,
            bytes_accessed=2 * (rows * depth + blocks * depth * width + len(operands) * blocks * rows * width),
            transcendentals=0,
        ),
    )(*operands)


def per_device(tokens, in_weight, filters, skip_gain, out_weight):
    swap = [(0, 1), (1, 0)]
    both_x = lax.ppermute(jnp.concatenate([tokens, out_weight]), "xhi", swap)
    tokens_x, weight_x = both_x[: tokens.shape[0]], both_x[tokens.shape[0] :]
    first = lax.axis_index("xhi") == 0
    pair = jnp.where(first, jnp.concatenate([tokens, tokens_x]), jnp.concatenate([tokens_x, tokens]))
    gathered = lax.all_gather(pair, "z", axis=0, tiled=True)
    same = lax.axis_index("xhi") == lax.axis_index("core")
    across = lax.ppermute(weight_x, "core", swap)
    chunk = jnp.where(same, out_weight, across)
    chips = axis_size(("xlo", "y"))
    spread = jnp.broadcast_to(chunk[None], (chips,) + chunk.shape)
    plane = lax.all_to_all(spread, ("xlo", "y"), 0, 0, tiled=True)
    gathered, plane = lax.optimization_barrier((gathered, plane))
    tok_dev = gathered.shape[0] // axis_size(SEQ)
    channels = in_weight.shape[2]
    taps_count = filters.shape[1]
    group_width = channels // filters.shape[0]
    summed = lax.psum_scatter(
        jnp.einsum("rf,sfc->rsc", gathered, in_weight, preferred_element_type=jnp.float32).astype(
            jnp.bfloat16
        ),
        SEQ,
        scatter_dimension=0,
        tiled=True,
    ).astype(jnp.float32)
    plane_other = lax.ppermute(plane, "core", swap)
    keep_w = jnp.swapaxes(jnp.where(same, plane, plane_other), 1, 2)
    recv_w = jnp.swapaxes(jnp.where(same, plane_other, plane), 1, 2)
    summed, keep_w, recv_w = lax.optimization_barrier((summed, keep_w, recv_w))
    query_rows = summed[:, 0].astype(jnp.bfloat16)
    key_rows = summed[:, 1].astype(jnp.bfloat16)
    value_rows = summed[:, 2].astype(jnp.bfloat16)
    product = (key_rows.astype(jnp.float32) * value_rows.astype(jnp.float32)).astype(jnp.bfloat16)
    previous = from_behind(product[tok_dev - (taps_count - 1) :], SEQ, 1)
    product_f = product.astype(jnp.float32)
    extended = jnp.concatenate([previous, product], axis=0)
    conv = toeplitz_conv(extended, filters)
    conv = conv + skip_gain[None, :] * product_f
    gated = (query_rows.astype(jnp.float32) * conv).astype(jnp.bfloat16)
    recv_g = lax.ppermute(gated, "xhi", swap)
    mine = out_proj(gated.T, keep_w)
    both = out_proj(recv_g.T, recv_w, mine)
    summed = lax.psum_scatter(both, "z", scatter_dimension=0, tiled=True)[0]
    return summed.T


def solution(mesh):
    n_seq, n_ten = mesh.devices.shape
    fine = Mesh(mesh.devices.reshape(2, 4, 2, n_ten // 2, 2), SEQ + TEN)
    placed = (
        P(TEN, SEQ),
        P(None, SEQ, TEN),
        P(TEN, None),
        P(TEN),
        P(TEN, SEQ),
    )
    return jax.shard_map(
        per_device, mesh=fine, in_specs=placed, out_specs=P(SEQ, TEN), check_vma=False
    )
```

```python
import jax
import jax.numpy as jnp
from jax import lax
from jax.experimental import pallas as pl
from jax.experimental.pallas import tpu as pltpu
from jax.sharding import Mesh, PartitionSpec as P


SEQ = ("xlo", "y", "core")
TEN = ("z", "xhi")


def axis_size(names):
    size = 1
    for name in names:
        size *= lax.axis_size(name)
    return size


def from_behind(x, axis, by):
    peers = axis_size(axis)
    pairs = [(i, i + by) for i in range(peers) if 0 <= i + by < peers]
    return lax.ppermute(x, axis, pairs)


def toeplitz_conv(ext, filters):
    groups, taps = filters.shape
    rows, channels = ext.shape
    tok = rows - (taps - 1)
    gw = channels // groups
    nblk = tok // taps
    extp = jnp.concatenate([ext, jnp.zeros((1, channels), ext.dtype)], axis=0)
    blocks = extp.reshape(nblk + 1, taps, groups, gw)
    win = jnp.concatenate([blocks[:-1], blocks[1:]], axis=1)
    w = jnp.pad(filters[:, ::-1], ((0, 0), (0, taps + 1)))
    toe = jnp.tile(w, (1, taps))[:, : taps * 2 * taps].reshape(groups, taps, 2 * taps)
    hi = toe.astype(jnp.bfloat16)
    lo = (toe - hi.astype(jnp.float32)).astype(jnp.bfloat16)
    both = jnp.concatenate([hi, lo], axis=2)
    twice = jnp.concatenate([win, win], axis=1)
    out = jnp.einsum("gts,isgc->itgc", both, twice, preferred_element_type=jnp.float32)
    return out.reshape(tok, channels)


def out_proj_kernel(gt_ref, w_ref, *rest):
    out_ref = rest[-1]
    step, width, depth = w_ref.shape
    res = jnp.dot(w_ref[...].reshape(step * width, depth), gt_ref[...], preferred_element_type=jnp.float32)
    res = res.reshape(step, width, gt_ref.shape[1])
    if len(rest) == 2:
        res = res + rest[0][...].astype(jnp.float32)
    out_ref[...] = res.astype(out_ref.dtype)


def out_proj(gated_t, weight_t, acc=None, per_step=4):
    depth, rows = gated_t.shape
    blocks, width, _ = weight_t.shape
    block = pl.BlockSpec((per_step, width, rows), lambda i: (i, 0, 0))
    specs = [pl.BlockSpec((depth, rows), lambda i: (0, 0)), pl.BlockSpec((per_step, width, depth), lambda i: (i, 0, 0))]
    operands = [gated_t, weight_t]
    if acc is not None:
        specs.append(block)
        operands.append(acc)
    return pl.pallas_call(
        out_proj_kernel,
        out_shape=jax.ShapeDtypeStruct((blocks, width, rows), jnp.bfloat16),
        grid=(blocks // per_step,),
        in_specs=specs,
        out_specs=block,
        cost_estimate=pl.CostEstimate(
            flops=2 * rows * depth * width * blocks,
            bytes_accessed=2 * (rows * depth + blocks * depth * width + len(operands) * blocks * rows * width),
            transcendentals=0,
        ),
    )(*operands)


def per_device(tokens, in_weight, filters, skip_gain, out_weight):
    swap = [(0, 1), (1, 0)]
    tokens_x = lax.ppermute(tokens, "xhi", swap)
    weight_x = lax.ppermute(out_weight, ("core", "xhi"), [(1, 0), (2, 3)])
    first = lax.axis_index("xhi") == 0
    pair = jnp.where(first, jnp.concatenate([tokens, tokens_x]), jnp.concatenate([tokens_x, tokens]))
    gathered = lax.all_gather(pair, "z", axis=0, tiled=True)
    same = lax.axis_index("xhi") == lax.axis_index("core")
    across = lax.ppermute(weight_x, "core", swap)
    chunk = jnp.where(same, out_weight, across)
    chips = axis_size(("xlo", "y"))
    spread = jnp.broadcast_to(chunk[None], (chips,) + chunk.shape)
    plane = lax.all_to_all(spread, ("xlo", "y"), 0, 0, tiled=True)
    gathered, plane = lax.optimization_barrier((gathered, plane))
    tok_dev = gathered.shape[0] // axis_size(SEQ)
    channels = in_weight.shape[2]
    taps_count = filters.shape[1]
    group_width = channels // filters.shape[0]
    summed = lax.psum_scatter(
        jnp.einsum("rf,sfc->rsc", gathered, in_weight, preferred_element_type=jnp.float32).astype(
            jnp.bfloat16
        ),
        SEQ,
        scatter_dimension=0,
        tiled=True,
    ).astype(jnp.float32)
    plane_other = lax.ppermute(plane, "core", swap)
    keep_w = jnp.swapaxes(jnp.where(same, plane, plane_other), 1, 2)
    recv_w = jnp.swapaxes(jnp.where(same, plane_other, plane), 1, 2)
    summed, keep_w, recv_w = lax.optimization_barrier((summed, keep_w, recv_w))
    query_rows = summed[:, 0].astype(jnp.bfloat16)
    key_rows = summed[:, 1].astype(jnp.bfloat16)
    value_rows = summed[:, 2].astype(jnp.bfloat16)
    product = (key_rows.astype(jnp.float32) * value_rows.astype(jnp.float32)).astype(jnp.bfloat16)
    previous = from_behind(product[tok_dev - (taps_count - 1) :], SEQ, 1)
    product_f = product.astype(jnp.float32)
    extended = jnp.concatenate([previous, product], axis=0)
    conv = toeplitz_conv(extended, filters)
    conv = conv + skip_gain[None, :] * product_f
    gated = (query_rows.astype(jnp.float32) * conv).astype(jnp.bfloat16)
    recv_g = lax.ppermute(gated, "xhi", swap)
    mine = out_proj(gated.T, keep_w)
    both = out_proj(recv_g.T, recv_w, mine)
    summed = lax.psum_scatter(both, "z", scatter_dimension=0, tiled=True)[0]
    return summed.T


def solution(mesh):
    n_seq, n_ten = mesh.devices.shape
    fine = Mesh(mesh.devices.reshape(2, 4, 2, n_ten // 2, 2), SEQ + TEN)
    placed = (
        P(TEN, SEQ),
        P(None, SEQ, TEN),
        P(TEN, None),
        P(TEN),
        P(TEN, SEQ),
    )
    return jax.shard_map(
        per_device, mesh=fine, in_specs=placed, out_specs=P(SEQ, TEN), check_vma=False
    )
```

```python
import jax
import jax.numpy as jnp
from jax import lax
from jax.experimental import pallas as pl
from jax.experimental.pallas import tpu as pltpu
from jax.sharding import Mesh, PartitionSpec as P


SEQ = ("xlo", "y", "core")
TEN = ("z", "xhi")


def axis_size(names):
    size = 1
    for name in names:
        size *= lax.axis_size(name)
    return size


def from_behind(x, axis, by):
    peers = axis_size(axis)
    pairs = [(i, i + by) for i in range(peers) if 0 <= i + by < peers]
    return lax.ppermute(x, axis, pairs)


def toeplitz_conv(ext, filters):
    groups, taps = filters.shape
    rows, channels = ext.shape
    tok = rows - (taps - 1)
    gw = channels // groups
    nblk = tok // taps
    extp = jnp.concatenate([ext, jnp.zeros((1, channels), ext.dtype)], axis=0)
    blocks = extp.reshape(nblk + 1, taps, groups, gw)
    win = jnp.concatenate([blocks[:-1], blocks[1:]], axis=1)
    w = jnp.pad(filters[:, ::-1], ((0, 0), (0, taps + 1)))
    toe = jnp.tile(w, (1, taps))[:, : taps * 2 * taps].reshape(groups, taps, 2 * taps)
    hi = toe.astype(jnp.bfloat16)
    lo = (toe - hi.astype(jnp.float32)).astype(jnp.bfloat16)
    both = jnp.concatenate([hi, lo], axis=2)
    twice = jnp.concatenate([win, win], axis=1)
    out = jnp.einsum("gts,isgc->itgc", both, twice, preferred_element_type=jnp.float32)
    return out.reshape(tok, channels)


def out_proj_kernel(gt_ref, w_ref, *rest):
    out_ref = rest[-1]
    step, width, depth = w_ref.shape
    res = jnp.dot(w_ref[...].reshape(step * width, depth), gt_ref[...], preferred_element_type=jnp.float32)
    res = res.reshape(step, width, gt_ref.shape[1])
    if len(rest) == 2:
        res = res + rest[0][...].astype(jnp.float32)
    out_ref[...] = res.astype(out_ref.dtype)


def out_proj(gated_t, weight_t, acc=None, per_step=4):
    depth, rows = gated_t.shape
    blocks, width, _ = weight_t.shape
    block = pl.BlockSpec((per_step, width, rows), lambda i: (i, 0, 0))
    specs = [pl.BlockSpec((depth, rows), lambda i: (0, 0)), pl.BlockSpec((per_step, width, depth), lambda i: (i, 0, 0))]
    operands = [gated_t, weight_t]
    if acc is not None:
        specs.append(block)
        operands.append(acc)
    return pl.pallas_call(
        out_proj_kernel,
        out_shape=jax.ShapeDtypeStruct((blocks, width, rows), jnp.bfloat16),
        grid=(blocks // per_step,),
        in_specs=specs,
        out_specs=block,
        cost_estimate=pl.CostEstimate(
            flops=2 * rows * depth * width * blocks,
            bytes_accessed=2 * (rows * depth + blocks * depth * width + len(operands) * blocks * rows * width),
            transcendentals=0,
        ),
    )(*operands)


def per_device(tokens, in_weight, filters, skip_gain, out_weight):
    swap = [(0, 1), (1, 0)]
    tokens_x = lax.ppermute(tokens, "xhi", swap)
    weight_x = lax.ppermute(out_weight, ("core", "xhi"), [(1, 0), (2, 3)])
    rows = tokens.shape[0]
    ring = jnp.concatenate([tokens_x, tokens, tokens_x])
    pair = lax.dynamic_slice_in_dim(ring, rows * (1 - lax.axis_index("xhi")), 2 * rows, 0)
    gathered = lax.all_gather(pair, "z", axis=0, tiled=True)
    same = lax.axis_index("xhi") == lax.axis_index("core")
    across = lax.ppermute(weight_x, "core", swap)
    chunk = jnp.where(same, out_weight, across)
    chips = axis_size(("xlo", "y"))
    spread = jnp.broadcast_to(chunk[None], (chips,) + chunk.shape)
    plane = lax.all_to_all(spread, ("xlo", "y"), 0, 0, tiled=True)
    gathered, plane = lax.optimization_barrier((gathered, plane))
    tok_dev = gathered.shape[0] // axis_size(SEQ)
    channels = in_weight.shape[2]
    taps_count = filters.shape[1]
    group_width = channels // filters.shape[0]
    summed = lax.psum_scatter(
        jnp.einsum("rf,sfc->rsc", gathered, in_weight, preferred_element_type=jnp.float32).astype(
            jnp.bfloat16
        ),
        SEQ,
        scatter_dimension=0,
        tiled=True,
    ).astype(jnp.float32)
    plane_other = lax.ppermute(plane, "core", swap)
    keep_w = jnp.swapaxes(jnp.where(same, plane, plane_other), 1, 2)
    recv_w = jnp.swapaxes(jnp.where(same, plane_other, plane), 1, 2)
    summed, keep_w, recv_w = lax.optimization_barrier((summed, keep_w, recv_w))
    query_rows = summed[:, 0].astype(jnp.bfloat16)
    key_rows = summed[:, 1].astype(jnp.bfloat16)
    value_rows = summed[:, 2].astype(jnp.bfloat16)
    product = (key_rows.astype(jnp.float32) * value_rows.astype(jnp.float32)).astype(jnp.bfloat16)
    previous = from_behind(product[tok_dev - (taps_count - 1) :], SEQ, 1)
    product_f = product.astype(jnp.float32)
    extended = jnp.concatenate([previous, product], axis=0)
    conv = toeplitz_conv(extended, filters)
    conv = conv + skip_gain[None, :] * product_f
    gated = (query_rows.astype(jnp.float32) * conv).astype(jnp.bfloat16)
    recv_g = lax.ppermute(gated, "xhi", swap)
    mine = out_proj(gated.T, keep_w)
    both = out_proj(recv_g.T, recv_w, mine)
    summed = lax.psum_scatter(both, "z", scatter_dimension=0, tiled=True)[0]
    return summed.T


def solution(mesh):
    n_seq, n_ten = mesh.devices.shape
    fine = Mesh(mesh.devices.reshape(2, 4, 2, n_ten // 2, 2), SEQ + TEN)
    placed = (
        P(TEN, SEQ),
        P(None, SEQ, TEN),
        P(TEN, None),
        P(TEN),
        P(TEN, SEQ),
    )
    return jax.shard_map(
        per_device, mesh=fine, in_specs=placed, out_specs=P(SEQ, TEN), check_vma=False
    )
```

```python
import jax
import jax.numpy as jnp
from jax import lax
from jax.experimental import pallas as pl
from jax.experimental.pallas import tpu as pltpu
from jax.sharding import Mesh, PartitionSpec as P


SEQ = ("xlo", "y", "core")
TEN = ("z", "xhi")


def axis_size(names):
    size = 1
    for name in names:
        size *= lax.axis_size(name)
    return size


def from_behind(x, axis, by):
    peers = axis_size(axis)
    pairs = [(i, i + by) for i in range(peers) if 0 <= i + by < peers]
    return lax.ppermute(x, axis, pairs)


def toeplitz_conv(ext, filters):
    groups, taps = filters.shape
    rows, channels = ext.shape
    tok = rows - (taps - 1)
    gw = channels // groups
    nblk = tok // taps
    extp = jnp.concatenate([ext, jnp.zeros((1, channels), ext.dtype)], axis=0)
    blocks = extp.reshape(nblk + 1, taps, groups, gw)
    win = jnp.concatenate([blocks[:-1], blocks[1:]], axis=1)
    w = jnp.pad(filters[:, ::-1], ((0, 0), (0, taps + 1)))
    toe = jnp.tile(w, (1, taps))[:, : taps * 2 * taps].reshape(groups, taps, 2 * taps)
    hi = toe.astype(jnp.bfloat16)
    lo = (toe - hi.astype(jnp.float32)).astype(jnp.bfloat16)
    both = jnp.concatenate([hi, lo], axis=2)
    twice = jnp.concatenate([win, win], axis=1)
    out = jnp.einsum("gts,isgc->itgc", both, twice, preferred_element_type=jnp.float32)
    return out.reshape(tok, channels)


def out_proj_kernel(gt_ref, w_ref, *rest):
    out_ref = rest[-1]
    step, width, depth = w_ref.shape
    res = jnp.dot(w_ref[...].reshape(step * width, depth), gt_ref[...], preferred_element_type=jnp.float32)
    res = res.reshape(step, width, gt_ref.shape[1])
    if len(rest) == 2:
        res = res + rest[0][...].astype(jnp.float32)
        for jj in range(step):
            out_ref[jj] = res[jj].T.astype(out_ref.dtype)
    else:
        out_ref[...] = res.astype(out_ref.dtype)


def out_proj(gated_t, weight_t, acc=None, per_step=4):
    depth, rows = gated_t.shape
    blocks, width, _ = weight_t.shape
    block = pl.BlockSpec((per_step, width, rows), lambda i: (i, 0, 0))
    shape = (blocks, width, rows)
    out_block = block
    if acc is not None:
        shape = (blocks, rows, width)
        out_block = pl.BlockSpec((per_step, rows, width), lambda i: (i, 0, 0))
    specs = [pl.BlockSpec((depth, rows), lambda i: (0, 0)), pl.BlockSpec((per_step, width, depth), lambda i: (i, 0, 0))]
    operands = [gated_t, weight_t]
    if acc is not None:
        specs.append(block)
        operands.append(acc)
    return pl.pallas_call(
        out_proj_kernel,
        out_shape=jax.ShapeDtypeStruct(shape, jnp.bfloat16),
        grid=(blocks // per_step,),
        in_specs=specs,
        out_specs=out_block,
        cost_estimate=pl.CostEstimate(
            flops=2 * rows * depth * width * blocks,
            bytes_accessed=2 * (rows * depth + blocks * depth * width + len(operands) * blocks * rows * width),
            transcendentals=0,
        ),
    )(*operands)


def per_device(tokens, in_weight, filters, skip_gain, out_weight):
    swap = [(0, 1), (1, 0)]
    tokens_x = lax.ppermute(tokens, "xhi", swap)
    weight_x = lax.ppermute(out_weight, ("core", "xhi"), [(1, 0), (2, 3)])
    rows = tokens.shape[0]
    ring = jnp.concatenate([tokens_x, tokens, tokens_x])
    pair = lax.dynamic_slice_in_dim(ring, rows * (1 - lax.axis_index("xhi")), 2 * rows, 0)
    gathered = lax.all_gather(pair, "z", axis=0, tiled=True)
    same = lax.axis_index("xhi") == lax.axis_index("core")
    across = lax.ppermute(weight_x, "core", swap)
    chunk = jnp.where(same, out_weight, across)
    chips = axis_size(("xlo", "y"))
    spread = jnp.broadcast_to(chunk[None], (chips,) + chunk.shape)
    plane = lax.all_to_all(spread, ("xlo", "y"), 0, 0, tiled=True)
    gathered, plane = lax.optimization_barrier((gathered, plane))
    tok_dev = gathered.shape[0] // axis_size(SEQ)
    channels = in_weight.shape[2]
    taps_count = filters.shape[1]
    group_width = channels // filters.shape[0]
    summed = lax.psum_scatter(
        jnp.einsum("rf,sfc->rsc", gathered, in_weight, preferred_element_type=jnp.float32).astype(
            jnp.bfloat16
        ),
        SEQ,
        scatter_dimension=0,
        tiled=True,
    ).astype(jnp.float32)
    plane_other = lax.ppermute(plane, "core", swap)
    keep_w = jnp.swapaxes(jnp.where(same, plane, plane_other), 1, 2)
    recv_w = jnp.swapaxes(jnp.where(same, plane_other, plane), 1, 2)
    summed, keep_w, recv_w = lax.optimization_barrier((summed, keep_w, recv_w))
    query_rows = summed[:, 0].astype(jnp.bfloat16)
    key_rows = summed[:, 1].astype(jnp.bfloat16)
    value_rows = summed[:, 2].astype(jnp.bfloat16)
    product = (key_rows.astype(jnp.float32) * value_rows.astype(jnp.float32)).astype(jnp.bfloat16)
    previous = from_behind(product[tok_dev - (taps_count - 1) :], SEQ, 1)
    product_f = product.astype(jnp.float32)
    extended = jnp.concatenate([previous, product], axis=0)
    conv = toeplitz_conv(extended, filters)
    conv = conv + skip_gain[None, :] * product_f
    gated = (query_rows.astype(jnp.float32) * conv).astype(jnp.bfloat16)
    recv_g = lax.ppermute(gated, "xhi", swap)
    mine = out_proj(gated.T, keep_w)
    both = out_proj(recv_g.T, recv_w, mine)
    summed = lax.psum_scatter(both, "z", scatter_dimension=0, tiled=True)[0]
    return summed


def solution(mesh):
    n_seq, n_ten = mesh.devices.shape
    fine = Mesh(mesh.devices.reshape(2, 4, 2, n_ten // 2, 2), SEQ + TEN)
    placed = (
        P(TEN, SEQ),
        P(None, SEQ, TEN),
        P(TEN, None),
        P(TEN),
        P(TEN, SEQ),
    )
    return jax.shard_map(
        per_device, mesh=fine, in_specs=placed, out_specs=P(SEQ, TEN), check_vma=False
    )
```

```python
import jax
import jax.numpy as jnp
from jax import lax
from jax.experimental import pallas as pl
from jax.experimental.pallas import tpu as pltpu
from jax.sharding import Mesh, PartitionSpec as P


SEQ = ("xlo", "y", "core")
TEN = ("z", "xhi")


def axis_size(names):
    size = 1
    for name in names:
        size *= lax.axis_size(name)
    return size


def from_behind(x, axis, by):
    peers = axis_size(axis)
    pairs = [(i, i + by) for i in range(peers) if 0 <= i + by < peers]
    return lax.ppermute(x, axis, pairs)


def toeplitz_conv(ext, filters):
    groups, taps = filters.shape
    rows, channels = ext.shape
    tok = rows - (taps - 1)
    gw = channels // groups
    nblk = tok // taps
    extp = jnp.concatenate([ext, jnp.zeros((1, channels), ext.dtype)], axis=0)
    blocks = extp.reshape(nblk + 1, taps, groups, gw)
    win = jnp.concatenate([blocks[:-1], blocks[1:]], axis=1)
    w = jnp.pad(filters[:, ::-1], ((0, 0), (0, taps + 1)))
    toe = jnp.tile(w, (1, taps))[:, : taps * 2 * taps].reshape(groups, taps, 2 * taps)
    hi = toe.astype(jnp.bfloat16)
    lo = (toe - hi.astype(jnp.float32)).astype(jnp.bfloat16)
    both = jnp.concatenate([hi, lo], axis=2)
    twice = jnp.concatenate([win, win], axis=1)
    out = jnp.einsum("gts,isgc->itgc", both, twice, preferred_element_type=jnp.float32)
    return out.reshape(tok, channels)


def out_proj_kernel(gt_ref, w_ref, *rest):
    out_ref = rest[-1]
    step, width, depth = w_ref.shape
    res = jnp.dot(w_ref[...].reshape(step * width, depth), gt_ref[...], preferred_element_type=jnp.float32)
    res = res.reshape(step, width, gt_ref.shape[1])
    if len(rest) == 2:
        res = res + rest[0][...].astype(jnp.float32)
        for jj in range(step):
            out_ref[jj] = res[jj].T.astype(out_ref.dtype)
    else:
        out_ref[...] = res.astype(out_ref.dtype)


def out_proj(gated_t, weight_t, acc=None, per_step=2):
    depth, rows = gated_t.shape
    blocks, width, _ = weight_t.shape
    block = pl.BlockSpec((per_step, width, rows), lambda i: (i, 0, 0))
    shape = (blocks, width, rows)
    out_block = block
    if acc is not None:
        shape = (blocks, rows, width)
        out_block = pl.BlockSpec((per_step, rows, width), lambda i: (i, 0, 0))
    specs = [pl.BlockSpec((depth, rows), lambda i: (0, 0)), pl.BlockSpec((per_step, width, depth), lambda i: (i, 0, 0))]
    operands = [gated_t, weight_t]
    if acc is not None:
        specs.append(block)
        operands.append(acc)
    return pl.pallas_call(
        out_proj_kernel,
        out_shape=jax.ShapeDtypeStruct(shape, jnp.bfloat16),
        grid=(blocks // per_step,),
        in_specs=specs,
        out_specs=out_block,
        cost_estimate=pl.CostEstimate(
            flops=2 * rows * depth * width * blocks,
            bytes_accessed=2 * (rows * depth + blocks * depth * width + len(operands) * blocks * rows * width),
            transcendentals=0,
        ),
    )(*operands)


def per_device(tokens, in_weight, filters, skip_gain, out_weight):
    swap = [(0, 1), (1, 0)]
    tokens_x = lax.ppermute(tokens, "xhi", swap)
    weight_x = lax.ppermute(out_weight, ("core", "xhi"), [(1, 0), (2, 3)])
    rows = tokens.shape[0]
    ring = jnp.concatenate([tokens_x, tokens, tokens_x])
    pair = lax.dynamic_slice_in_dim(ring, rows * (1 - lax.axis_index("xhi")), 2 * rows, 0)
    gathered = lax.all_gather(pair, "z", axis=0, tiled=True)
    same = lax.axis_index("xhi") == lax.axis_index("core")
    across = lax.ppermute(weight_x, "core", swap)
    chunk = jnp.where(same, out_weight, across)
    chips = axis_size(("xlo", "y"))
    spread = jnp.broadcast_to(chunk[None], (chips,) + chunk.shape)
    plane = lax.all_to_all(spread, ("xlo", "y"), 0, 0, tiled=True)
    gathered, plane = lax.optimization_barrier((gathered, plane))
    tok_dev = gathered.shape[0] // axis_size(SEQ)
    channels = in_weight.shape[2]
    taps_count = filters.shape[1]
    group_width = channels // filters.shape[0]
    summed = lax.psum_scatter(
        jnp.einsum("rf,sfc->rsc", gathered, in_weight, preferred_element_type=jnp.float32).astype(
            jnp.bfloat16
        ),
        SEQ,
        scatter_dimension=0,
        tiled=True,
    ).astype(jnp.float32)
    plane_other = lax.ppermute(plane, "core", swap)
    keep_w = jnp.swapaxes(jnp.where(same, plane, plane_other), 1, 2)
    recv_w = jnp.swapaxes(jnp.where(same, plane_other, plane), 1, 2)
    summed, keep_w, recv_w = lax.optimization_barrier((summed, keep_w, recv_w))
    query_rows = summed[:, 0].astype(jnp.bfloat16)
    key_rows = summed[:, 1].astype(jnp.bfloat16)
    value_rows = summed[:, 2].astype(jnp.bfloat16)
    product = (key_rows.astype(jnp.float32) * value_rows.astype(jnp.float32)).astype(jnp.bfloat16)
    previous = from_behind(product[tok_dev - (taps_count - 1) :], SEQ, 1)
    product_f = product.astype(jnp.float32)
    extended = jnp.concatenate([previous, product], axis=0)
    conv = toeplitz_conv(extended, filters)
    conv = conv + skip_gain[None, :] * product_f
    gated = (query_rows.astype(jnp.float32) * conv).astype(jnp.bfloat16)
    recv_g = lax.ppermute(gated, "xhi", swap)
    mine = out_proj(gated.T, keep_w)
    both = out_proj(recv_g.T, recv_w, mine)
    summed = lax.psum_scatter(both, "z", scatter_dimension=0, tiled=True)[0]
    return summed


def solution(mesh):
    n_seq, n_ten = mesh.devices.shape
    fine = Mesh(mesh.devices.reshape(2, 4, 2, n_ten // 2, 2), SEQ + TEN)
    placed = (
        P(TEN, SEQ),
        P(None, SEQ, TEN),
        P(TEN, None),
        P(TEN),
        P(TEN, SEQ),
    )
    return jax.shard_map(
        per_device, mesh=fine, in_specs=placed, out_specs=P(SEQ, TEN), check_vma=False
    )
```
